128 devices in a mesh: req: 8 (over y, core), row: 4 (over z), col: 4 (over x).
Axes of the slice: x: 4, y: 4, z: 4, core: 2. Of those that a mesh axis runs over, the one named last changes fastest.
Arguments:
- tokens: bfloat16 [32, 64, 2048], P('req', None, ('row', 'col')), may hold values from -6 to 6
- order: int32 [32], replicated, may hold values from 0 to 31, each once
- lengths: int32 [32], P('req'), may hold values from 1 to 8184, as said below
- parents: int32 [32, 64], P('req'), may hold values from 0 to 62, as said below
- path: int32 [32, 8], P('req'), may hold values from 0 to 56, as said below
- cache_keys: bfloat16 [32, 8192, 1024], P('req', ('row', 'col')), may hold values from -288 to 288
- cache_values: bfloat16 [32, 8192, 1024], P('req', ('row', 'col')), may hold values from -6 to 6
- attn_gain: float32 [2048], P(('row', 'col')), may hold values from 0.25 to 1.75
- qkv_weight: bfloat16 [2048, 4096], P(('row', 'col')), may hold values from -0.1875 to 0.1875
- out_weight: bfloat16 [2048, 2048], P(None, ('row', 'col')), may hold values from -0.125 to 0.125
- ffn_gain: float32 [2048], P(('row', 'col')), may hold values from 0.25 to 1.75
- gate_weight: bfloat16 [2048, 8192], P('row', 'col'), may hold values from -0.125 to 0.125
- up_weight: bfloat16 [2048, 8192], P('row', 'col'), may hold values from -0.125 to 0.125
- down_weight: bfloat16 [8192, 2048], P('col', 'row'), may hold values from -0.0625 to 0.0625
Outputs:
- hidden_out: bfloat16 [32, 64, 2048], P('req', None, ('row', 'col'))
- new_keys: bfloat16 [32, 8, 1024], P('req')
- new_values: bfloat16 [32, 8, 1024], P('req')
The draws below stay inside these ranges and needn't reach their ends.
Inputs may be any that keep to these rules, and one draw needn't show every extreme that they name: order lists every request once; slot s serves request order[s]. `lengths`: some slot has exactly 8184 cached tokens. parents[s, 0] = 0; for i >= 1, parents[s, i] lies between max(0, i - 8) and i - 1. path[s, 0] = 0 and parents[s, path[s, a + 1]] = path[s, a].
All inputs are finite; a program needn't handle non-finite values.
Results may differ from the reference program's by a relative error of at most 0.012.
The reference program's roundings to bfloat16 on the way (of `slot_tokens`, `normed`, `queries`, `attended`, `middle`, `normed_two`, `hidden` and `final`) count: a program that leaves them out, or rounds other values in their place, can miss the bound.
Values may be sent and summed in bfloat16 or wider, within the bound.
No kernel may reach another device: no remote copies, remote signals or barrier semaphores. Data moves between devices by JAX's collectives and lax.ppermute only.
A program may use at most 192 MiB of HBM per device.

```python
import math
import jax
import jax.numpy as jnp
from jax import lax

D = 2048
FF = 8192
HEADS = 16
KV_HEADS = 8
HEAD_DIM = 128
DRAFT = 64
ACC = 8
BRANCH = 8
CACHE = 8192
REQS = 32
QKV = 4096
KVD = 1024


def draw_tokens(key, part):
    feature_steps = jnp.arange(D, dtype=jnp.float32) / max(D - 1, 1)
    feature_scales = 0.5 * jnp.exp(feature_steps * math.log(3.0))
    drawn = jnp.clip(jax.random.normal(key, (REQS, DRAFT, D), jnp.float32), -4.0, 4.0)
    return (drawn * feature_scales).astype(jnp.bfloat16)


def draw_lengths(key, part):
    top_length = CACHE - ACC
    first_key, second_key, third_key = jax.random.split(key, 3)
    first_draw = jax.random.randint(first_key, (REQS,), 0, top_length)
    second_draw = jax.random.randint(second_key, (REQS,), 0, top_length)
    skewed = 1 + first_draw * second_draw // max(top_length - 1, 1)
    chosen = jax.random.randint(third_key, (), 0, REQS)
    return jnp.where(jnp.arange(REQS) == chosen, top_length, skewed).astype(jnp.int32)


def tree_draw(key):
    tree_key = jax.random.fold_in(key, 11)
    parent_key, end_key, pick_key = jax.random.split(tree_key, 3)
    node_ids = jnp.arange(DRAFT, dtype=jnp.int32)
    lowest = jnp.maximum(node_ids - BRANCH, 0)
    spans = jnp.maximum(node_ids - lowest, 1)
    raw_bits = jax.random.randint(parent_key, (REQS, DRAFT), 0, 1 << 20)
    parents = (lowest + raw_bits % spans).astype(jnp.int32)
    top_node = min((ACC - 1) * BRANCH, DRAFT - 1)
    forced_nodes = [0] + [top_node - (ACC - 1 - step) * BRANCH for step in range(1, ACC)]
    picked = jax.random.randint(pick_key, (), 0, REQS)
    is_picked = jnp.arange(REQS, dtype=jnp.int32) == picked
    for step in range(1, ACC):
        spot = is_picked[:, None] & (node_ids == forced_nodes[step])[None, :]
        parents = jnp.where(spot, forced_nodes[step - 1], parents).astype(jnp.int32)
    first_end = max((ACC - 2) * BRANCH + 1, 1)
    current = jax.random.randint(end_key, (REQS,), first_end, DRAFT).astype(jnp.int32)
    chain_list = []
    for turn_index in range(DRAFT):
        chain_list.append(current)
        current = jnp.take_along_axis(parents, current[:, None], axis=1)[:, 0]
    chain = jnp.stack(chain_list, axis=1)
    depth = jnp.sum((chain != 0).astype(jnp.int32), axis=1)
    steps_back = depth[:, None] - jnp.arange(ACC, dtype=jnp.int32)[None, :]
    path = jnp.take_along_axis(chain, steps_back, axis=1)
    forced_path = jnp.array(forced_nodes, dtype=jnp.int32)[None, :]
    path = jnp.where(is_picked[:, None], forced_path, path)
    return (parents, path.astype(jnp.int32))


def draw_parents(key, part):
    return tree_draw(key)[0]


def draw_path(key, part):
    return tree_draw(key)[1]


def draw_cache_keys(key, part):
    base_key = jax.random.fold_in(key, 0)
    key_shape = (REQS, CACHE, KVD)
    drawn_keys = jnp.clip(jax.random.normal(base_key, key_shape, jnp.float32), -6.0, 6.0)
    return drawn_keys.astype(jnp.bfloat16)


def spiked(values, key, source, target, shards_of, factor):
    owner, partner = [(jnp.arange(values.shape[axis_at]) // (values.shape[axis_at] // shards_of)).reshape([-1 if axis == axis_at else 1 for axis in range(values.ndim)]) for axis_at in (source, target)]
    chosen = jax.random.permutation(key, shards_of)[partner]
    strong = (owner == chosen) | (owner == (partner + shards_of // 2) % shards_of)
    return jnp.where(strong, factor * values, values)


def steps_of(own_key, dims, cuts, smallest, top_value):
    loudness = 1.0
    for axis_at, shards_of in cuts:
        heights = jax.random.uniform(jax.random.fold_in(jax.random.fold_in(own_key, 6), axis_at), (shards_of,), jnp.float32, smallest / len(cuts), top_value / len(cuts))
        loudness = loudness * jnp.repeat(jnp.exp(heights), dims[axis_at] // shards_of).reshape((-1,) + (1,) * (len(dims) - 1 - axis_at))
    return loudness


def normal_values(rng, dims, width, reach, pieces=(), kind=jnp.bfloat16):
    result = width * jax.random.normal(rng, dims, jnp.float32)
    if pieces:
        result = result * steps_of(rng, dims, pieces, -0.22, 0.18)
    return jnp.clip(result, -reach, reach).astype(kind)


def heavy_noise(stream_key, dims, deviation, most, pieces, heavy, kind=jnp.bfloat16):
    values = deviation * jax.random.normal(stream_key, dims, jnp.float32)
    if pieces:
        values = values * steps_of(stream_key, dims, pieces, -0.22, 0.18)
    return jnp.clip(spiked(values, jax.random.fold_in(stream_key, 3), *heavy), -most, most).astype(kind)


def setup_inputs(seed: int = 0) -> dict:
    key_of = jax.random.split(jax.random.key(seed), 15)
    tokens = draw_tokens(jax.random.fold_in(key_of[14], 71), 0)
    order = jax.random.permutation(key_of[1], REQS).astype(jnp.int32)
    lengths = draw_lengths(jax.random.fold_in(key_of[14], 71), 0)
    parents = draw_parents(jax.random.fold_in(key_of[14], 71), 0)
    path = draw_path(jax.random.fold_in(key_of[14], 71), 0)
    cache_keys = draw_cache_keys(jax.random.fold_in(key_of[14], 71), 0)
    cache_values = normal_values(key_of[6], (REQS, CACHE, KVD), 1.0, 6.0, ((0, 8), (1, 16)))
    attn_gain = jnp.clip(1.0 + 0.15 * jax.random.normal(key_of[7], (D,), jnp.float32), 0.25, 1.75)
    qkv_weight = heavy_noise(key_of[8], (D, QKV), D ** -0.5, 0.1875, ((0, 16),), (0, 1, 16, 2.0))
    out_weight = normal_values(key_of[9], (HEADS * HEAD_DIM, D), (HEADS * HEAD_DIM) ** -0.5, 0.125, ((1, 16),))
    ffn_gain = jnp.clip(1.0 + 0.15 * jax.random.normal(key_of[10], (D,), jnp.float32), 0.25, 1.75)
    gate_weight = normal_values(key_of[11], (D, FF), D ** -0.5, 0.125, ((0, 4), (1, 4)))
    up_weight = normal_values(key_of[12], (D, FF), D ** -0.5, 0.125, ((0, 4), (1, 4)))
    down_weight = normal_values(key_of[13], (FF, D), FF ** -0.5, 0.0625, ((0, 4), (1, 4)))
    return dict(tokens=tokens, order=order, lengths=lengths, parents=parents, path=path, cache_keys=cache_keys, cache_values=cache_values, attn_gain=attn_gain, qkv_weight=qkv_weight, out_weight=out_weight, ffn_gain=ffn_gain, gate_weight=gate_weight, up_weight=up_weight, down_weight=down_weight)


rope_base = 1000000.0
norm_eps = 1e-05
masked_low = -1e+30

def rotary(head_values, positions):
    head_width = head_values.shape[-1]
    half_width = head_width // 2
    freqs = rope_base ** (-(jnp.arange(half_width, dtype=jnp.float32) * 2.0 / head_width))
    angles = positions.astype(jnp.float32)[..., None] * freqs
    cosine = jnp.cos(angles)[..., None, :]
    sine_part = jnp.sin(angles)[..., None, :]
    first_half = head_values[..., :half_width]
    second_half = head_values[..., half_width:]
    return jnp.concatenate([first_half * cosine - second_half * sine_part, second_half * cosine + first_half * sine_part], axis=-1)

def ancestry(parents):
    tree_size = parents.shape[1]
    node_ids = jnp.arange(tree_size, dtype=jnp.int32)
    walkers = jnp.broadcast_to(node_ids, parents.shape)

    def advance(turn_index, carried):
        found, current = carried
        found = jnp.maximum(found, (current[..., None] == node_ids).astype(jnp.int32))
        current = jnp.take_along_axis(parents, current, axis=1)
        return (found, current)
    found, walkers = lax.fori_loop(0, tree_size, advance, (jnp.zeros(parents.shape + (tree_size,), jnp.int32), walkers))
    return (found, lax.optimization_barrier(jnp.sum(found, axis=-1)) - 1)

def reference(tokens, order, lengths, parents, path, cache_keys, cache_values, attn_gain, qkv_weight, out_weight, ffn_gain, gate_weight, up_weight, down_weight):
    token_rows = REQS * DRAFT
    slot_tokens = jnp.take(tokens, order, axis=0).reshape(token_rows, D)
    residual = slot_tokens.astype(jnp.float32)
    normed = (residual * lax.rsqrt(lax.optimization_barrier(jnp.mean(residual * residual, axis=1, keepdims=True)) + norm_eps) * attn_gain).astype(jnp.bfloat16)
    mixed = jnp.dot(normed, qkv_weight, preferred_element_type=jnp.float32)
    ancestors, depth = ancestry(parents)
    positions = (lengths[:, None] + depth).reshape(token_rows)
    query_width = HEADS * HEAD_DIM
    group_size = HEADS // KV_HEADS
    queries = rotary(mixed[:, :query_width].reshape(token_rows, HEADS, HEAD_DIM), positions).astype(jnp.bfloat16)
    keys = rotary(mixed[:, query_width:query_width + KVD].reshape(token_rows, KV_HEADS, HEAD_DIM), positions).astype(jnp.bfloat16)
    values = mixed[:, query_width + KVD:].astype(jnp.bfloat16)
    queries = queries.reshape(REQS, DRAFT, KV_HEADS, group_size, HEAD_DIM)
    keys = keys.reshape(REQS, DRAFT, KV_HEADS, HEAD_DIM)
    values = values.reshape(REQS, DRAFT, KV_HEADS, HEAD_DIM)
    score_scale = 1.0 / math.sqrt(HEAD_DIM)

    def per_slot(items):
        slot_query, slot_keys, slot_values, slot_cache_keys, slot_cache_values, slot_ancestors, slot_length = items
        query_float = slot_query.astype(jnp.float32)
        cache_scores = jnp.einsum('tgrd,pgd->grtp', query_float, slot_cache_keys.reshape(CACHE, KV_HEADS, HEAD_DIM).astype(jnp.float32)) * score_scale
        tree_scores = jnp.einsum('tgrd,ugd->grtu', query_float, slot_keys.astype(jnp.float32)) * score_scale
        cache_alive = jnp.broadcast_to((jnp.arange(CACHE, dtype=jnp.int32) < slot_length)[None, :], (DRAFT, CACHE))
        alive_mask = jnp.concatenate([cache_alive, slot_ancestors > 0], axis=1)
        scores = jnp.where(alive_mask, jnp.concatenate([cache_scores, tree_scores], axis=-1), masked_low)
        row_max = lax.optimization_barrier(jnp.max(scores, axis=-1, keepdims=True))
        weights = jnp.where(alive_mask, jnp.exp(scores - row_max), 0.0)
        totals = lax.optimization_barrier(jnp.sum(weights, axis=-1))
        rounded = lax.optimization_barrier(weights.astype(jnp.bfloat16)).astype(jnp.float32)
        all_values = jnp.concatenate([slot_cache_values.reshape(CACHE, KV_HEADS, HEAD_DIM), slot_values], axis=0).astype(jnp.float32)
        numerator = jnp.einsum('grtp,pgd->grtd', rounded, all_values)
        attended_slot = (numerator / totals[..., None]).transpose(2, 0, 1, 3)
        return attended_slot.reshape(DRAFT, query_width).astype(jnp.bfloat16)
    attended = lax.map(per_slot, (queries, keys, values, cache_keys, cache_values, ancestors, lengths))
    attn_out = jnp.dot(attended.reshape(token_rows, query_width), out_weight, preferred_element_type=jnp.float32)
    middle = (residual + attn_out).astype(jnp.bfloat16)
    middle_float = middle.astype(jnp.float32)
    normed_two = (middle_float * lax.rsqrt(lax.optimization_barrier(jnp.mean(middle_float * middle_float, axis=1, keepdims=True)) + norm_eps) * ffn_gain).astype(jnp.bfloat16)
    gate = jnp.dot(normed_two, gate_weight, preferred_element_type=jnp.float32)
    up_proj = jnp.dot(normed_two, up_weight, preferred_element_type=jnp.float32)
    hidden = (jax.nn.silu(gate) * up_proj).astype(jnp.bfloat16)
    final = (middle_float + jnp.dot(hidden, down_weight, preferred_element_type=jnp.float32)).astype(jnp.bfloat16)
    final = final.reshape(REQS, DRAFT, D)
    hidden_out = jnp.zeros_like(final).at[order].set(final)
    new_keys = jnp.take_along_axis(keys.reshape(REQS, DRAFT, KVD), path[:, :, None], axis=1)
    new_values = jnp.take_along_axis(values.reshape(REQS, DRAFT, KVD), path[:, :, None], axis=1)
    return (hidden_out, new_keys, new_values)
```

```python
import math

import jax
import jax.numpy as jnp
from jax import lax
from jax.sharding import PartitionSpec as P

HEADS = 16
KV_HEADS = 8
HEAD_DIM = 128

rope_base = 1000000.0
norm_eps = 1e-05
masked_low = -1e30

GROUP = ("row", "col")


def gather_all(x, axis, n):
    spread = jnp.broadcast_to(x[None], (n,) + x.shape)
    return lax.all_to_all(spread, axis, 0, 0, tiled=True)


def scatter_sum(x, axis):
    return jnp.sum(lax.all_to_all(x, axis, 0, 0, tiled=True), axis=0)


def rotary(head_values, positions):
    head_width = head_values.shape[-1]
    half_width = head_width // 2
    freqs = rope_base ** (-(jnp.arange(half_width, dtype=jnp.float32) * 2.0 / head_width))
    angles = positions.astype(jnp.float32)[..., None] * freqs
    cosine = jnp.cos(angles)[..., None, :]
    sine_part = jnp.sin(angles)[..., None, :]
    first_half = head_values[..., :half_width]
    second_half = head_values[..., half_width:]
    return jnp.concatenate(
        [
            first_half * cosine - second_half * sine_part,
            second_half * cosine + first_half * sine_part,
        ],
        axis=-1,
    )


def ancestry(parents):
    tree_size = parents.shape[1]
    node_ids = jnp.arange(tree_size, dtype=jnp.int32)
    step_one = (parents[:, :, None] == node_ids[None, None, :]) | (
        node_ids[:, None] == node_ids[None, :]
    )[None, :, :]
    reach = step_one.astype(jnp.bfloat16)
    squarings = max(1, (tree_size - 1).bit_length())
    for turn_index in range(squarings):
        product = jnp.einsum("sij,sjk->sik", reach, reach, preferred_element_type=jnp.float32)
        reach = (product > 0.5).astype(jnp.bfloat16)
    found = (reach > 0.5).astype(jnp.int32)
    return (found, jnp.sum(found, axis=-1) - 1)


def local(
    tokens,
    order,
    lengths,
    parents,
    path,
    cache_keys,
    cache_values,
    attn_gain,
    qkv_weight,
    out_weight,
    ffn_gain,
    gate_weight,
    up_weight,
    down_weight,
):
    n_req = lax.axis_size("req")
    n_row = lax.axis_size("row")
    n_col = lax.axis_size("col")
    n_grp = n_row * n_col
    slot_count = lengths.shape[0]
    draft_size = parents.shape[1]
    local_width = tokens.shape[2]
    model_width = local_width * n_grp
    token_rows = slot_count * draft_size
    query_width = HEADS * HEAD_DIM
    kv_width = KV_HEADS * HEAD_DIM
    group_size = HEADS // KV_HEADS
    me = lax.axis_index(GROUP)
    row_index = lax.axis_index("row")

    group_index = lax.axis_index("req")
    every_token = gather_all(tokens, "req", n_req).reshape((-1,) + tokens.shape[1:])
    own_index = group_index * slot_count + jnp.arange(slot_count, dtype=jnp.int32)
    requests_here = jnp.take(order, own_index, axis=0)
    slot_tokens = jnp.take(every_token, requests_here, axis=0).reshape(token_rows, local_width)
    residual = slot_tokens.astype(jnp.float32)

    full_tokens = (
        gather_all(slot_tokens, GROUP, n_grp).transpose(1, 0, 2).reshape(token_rows, model_width)
    )
    gains = gather_all(jnp.stack([attn_gain, ffn_gain]), GROUP, n_grp)
    attn_gain_full = gains[:, 0, :].reshape(model_width)
    ffn_gain_full = gains[:, 1, :].reshape(model_width)
    mixed_total = qkv_weight.shape[1]
    share_width = mixed_total // n_grp
    weight_cols = lax.all_to_all(
        qkv_weight.reshape(local_width, n_grp, share_width).transpose(1, 0, 2),
        GROUP,
        0,
        0,
        tiled=True,
    ).reshape(model_width, share_width)

    full_float = full_tokens.astype(jnp.float32)
    squares = jnp.sum(full_float * full_float, axis=1)
    normed = (
        full_float * lax.rsqrt(squares / model_width + norm_eps)[:, None] * attn_gain_full
    ).astype(jnp.bfloat16)
    mixed_share = jnp.dot(normed, weight_cols, preferred_element_type=jnp.float32)

    ancestors, depth = ancestry(parents)
    positions = (lengths[:, None] + depth).reshape(token_rows)
    heads_here = share_width // HEAD_DIM
    rotated = rotary(mixed_share.reshape(token_rows, heads_here, HEAD_DIM), positions).reshape(
        token_rows, share_width
    )
    share_start = me * share_width
    rotated_width = query_width + kv_width
    share_out = jnp.where(share_start < rotated_width, rotated, mixed_share).astype(jnp.bfloat16)
    mixed_all = (
        gather_all(share_out, GROUP, n_grp).transpose(1, 0, 2).reshape(token_rows, mixed_total)
    )

    queries = mixed_all[:, :query_width].reshape(
        slot_count, draft_size, KV_HEADS, group_size, HEAD_DIM
    )
    keys = mixed_all[:, query_width : query_width + kv_width]
    values = mixed_all[:, query_width + kv_width :]

    cache_rows = cache_keys.shape[1]
    cache_start = me * cache_rows
    key_blocks = cache_keys.reshape(slot_count, cache_rows, KV_HEADS, HEAD_DIM)
    value_blocks = cache_values.reshape(slot_count, cache_rows, KV_HEADS, HEAD_DIM)
    score_scale = 1.0 / math.sqrt(HEAD_DIM)
    cache_scores = (
        jnp.einsum("stgrd,spgd->grstp", queries, key_blocks, preferred_element_type=jnp.float32)
        * score_scale
    )
    alive = ((cache_start + jnp.arange(cache_rows, dtype=jnp.int32))[None, :] < lengths[:, None])[
        None, None, :, None, :
    ]
    cache_max = jnp.max(jnp.where(alive, cache_scores, masked_low), axis=-1)
    weights = jnp.where(alive, jnp.exp(cache_scores - cache_max[..., None]), 0.0)
    cache_total = jnp.sum(weights, axis=-1)
    cache_numer = jnp.einsum(
        "grstp,spgd->grstd",
        weights.astype(jnp.bfloat16),
        value_blocks,
        preferred_element_type=jnp.float32,
    )
    stat_rows = token_rows // HEAD_DIM
    packed = jnp.concatenate(
        [
            cache_numer.reshape(HEADS, token_rows, HEAD_DIM),
            cache_max.reshape(HEADS, stat_rows, HEAD_DIM),
            cache_total.reshape(HEADS, stat_rows, HEAD_DIM),
        ],
        axis=1,
    )
    arrived = lax.all_to_all(packed, GROUP, 0, 0, tiled=True)
    part_numer = arrived[:, :token_rows, :]
    part_max = arrived[:, token_rows : token_rows + stat_rows, :].reshape(n_grp, token_rows)
    part_total = arrived[:, token_rows + stat_rows :, :].reshape(n_grp, token_rows)

    head = me
    kv_head = head // group_size
    head_query = lax.dynamic_slice_in_dim(mixed_all, head * HEAD_DIM, HEAD_DIM, axis=1)
    head_key = lax.dynamic_slice_in_dim(keys, kv_head * HEAD_DIM, HEAD_DIM, axis=1)
    head_value = lax.dynamic_slice_in_dim(values, kv_head * HEAD_DIM, HEAD_DIM, axis=1)
    tree_scores = (
        jnp.einsum(
            "std,sud->stu",
            head_query.reshape(slot_count, draft_size, HEAD_DIM),
            head_key.reshape(slot_count, draft_size, HEAD_DIM),
            preferred_element_type=jnp.float32,
        )
        * score_scale
    )
    tree_alive = ancestors > 0
    tree_max = jnp.max(jnp.where(tree_alive, tree_scores, masked_low), axis=-1)
    tree_weights = jnp.where(tree_alive, jnp.exp(tree_scores - tree_max[..., None]), 0.0)
    tree_total = jnp.sum(tree_weights, axis=-1).reshape(token_rows)
    tree_numer = jnp.einsum(
        "stu,sud->std",
        tree_weights.astype(jnp.bfloat16),
        head_value.reshape(slot_count, draft_size, HEAD_DIM),
        preferred_element_type=jnp.float32,
    ).reshape(token_rows, HEAD_DIM)
    tree_max = tree_max.reshape(token_rows)

    joint_max = jnp.maximum(jnp.max(part_max, axis=0), tree_max)
    part_factor = jnp.exp(part_max - joint_max)
    tree_factor = jnp.exp(tree_max - joint_max)
    joint_total = jnp.sum(part_total * part_factor, axis=0) + tree_total * tree_factor
    joint_numer = (
        jnp.sum(part_numer * part_factor[..., None], axis=0) + tree_numer * tree_factor[:, None]
    )
    attended_head = (joint_numer / joint_total[:, None]).astype(jnp.bfloat16)
    attended = (
        gather_all(attended_head, GROUP, n_grp).transpose(1, 0, 2).reshape(token_rows, query_width)
    )
    attn_out = jnp.dot(attended, out_weight, preferred_element_type=jnp.float32)
    middle = (residual + attn_out).astype(jnp.bfloat16)
    middle_float = middle.astype(jnp.float32)

    block_width = local_width * n_col
    middle_block = (
        gather_all(middle, "col", n_col).transpose(1, 0, 2).reshape(token_rows, block_width)
    )
    block_float = middle_block.astype(jnp.float32)
    squares_part = jnp.sum(block_float * block_float, axis=1)
    squares_two = jnp.sum(gather_all(squares_part, "row", n_row), axis=0)
    gain_block = lax.dynamic_slice_in_dim(ffn_gain_full, row_index * block_width, block_width)
    normed_two = (
        block_float * lax.rsqrt(squares_two / model_width + norm_eps)[:, None] * gain_block
    ).astype(jnp.bfloat16)
    gate_part = jnp.dot(normed_two, gate_weight, preferred_element_type=jnp.float32)
    up_part = jnp.dot(normed_two, up_weight, preferred_element_type=jnp.float32)
    hidden_cols = gate_part.shape[1]
    sub_cols = hidden_cols // n_row
    both = jnp.stack([gate_part, up_part]).reshape(2, token_rows, n_row, sub_cols)
    summed = scatter_sum(both.transpose(2, 0, 1, 3), "row")
    gate_sum = summed[0]
    up_sum = summed[1]
    hidden_sub = (jax.nn.silu(gate_sum) * up_sum).astype(jnp.bfloat16)
    hidden = (
        gather_all(hidden_sub, "row", n_row).transpose(1, 0, 2).reshape(token_rows, hidden_cols)
    )
    down_part = jnp.dot(hidden, down_weight, preferred_element_type=jnp.float32)
    down_share = scatter_sum(
        down_part.reshape(token_rows, n_col, local_width).transpose(1, 0, 2), "col"
    )
    final_rows = (
        (middle_float + down_share)
        .astype(jnp.bfloat16)
        .reshape(slot_count, draft_size, local_width)
    )
    every_final = gather_all(final_rows, "req", n_req).reshape((-1,) + final_rows.shape[1:])
    slot_ids = jnp.arange(order.shape[0], dtype=jnp.int32)
    matches = (order[:, None] == slot_ids[None, :]).astype(jnp.int32)
    inverse = jnp.sum(matches * slot_ids[:, None], axis=0)
    hidden_out = jnp.take(every_final, jnp.take(inverse, own_index, axis=0), axis=0)
    new_keys = jnp.take_along_axis(
        keys.reshape(slot_count, draft_size, kv_width), path[:, :, None], axis=1
    )
    new_values = jnp.take_along_axis(
        values.reshape(slot_count, draft_size, kv_width), path[:, :, None], axis=1
    )
    return (hidden_out, new_keys, new_values)


def solution(mesh):
    in_specs = (
        P("req", None, ("row", "col")),
        P(),
        P("req"),
        P("req", None),
        P("req", None),
        P("req", ("row", "col"), None),
        P("req", ("row", "col"), None),
        P(("row", "col")),
        P(("row", "col"), None),
        P(None, ("row", "col")),
        P(("row", "col")),
        P("row", "col"),
        P("row", "col"),
        P("col", "row"),
    )
    out_specs = (P("req", None, ("row", "col")), P("req", None, None), P("req", None, None))
    return jax.shard_map(local, mesh=mesh, in_specs=in_specs, out_specs=out_specs, check_vma=False)
```
